256 devices in a mesh: tm: 64 (over y, z, core), state: 4 (over x).
Axes of the slice: x: 4, y: 4, z: 8, core: 2. Of those that a mesh axis runs over, the one named last changes fastest.
Arguments:
- dynamics: float32 [512, 512], P('state'), may hold values from -1 to 1
- pattern: int32 [4, 4], replicated, may hold values from 0 to 1
- initial_mean: float32 [4, 512], replicated, may hold values from -6 to 6
- observed: float32 [1024, 4], P('tm'), may hold values from -6 to 6
- obs_index: int32 [1024], P('tm'), may hold values from 0 to 511
- obs_noise: float32 [1024], P('tm'), may hold values from 0.5 to 4
Outputs:
- filtered: float32 [1024, 4, 512], P('tm', 'state')
- smoothed: float32 [1024, 4, 512], P('tm', 'state')
The draws below stay inside these ranges and needn't reach their ends.
All inputs are finite; a program needn't handle non-finite values.
Results may differ from the reference program's by a relative error of at most 0.0003.
Values sent between devices are 32-bit elements; how exact they have to be, the bound alone decides.
No kernel may reach another device: no remote copies, remote signals or barrier semaphores. Data moves between devices by JAX's collectives and lax.ppermute only.
A program may use at most 256 MiB of HBM per device.

```python
import math
import jax
import jax.numpy as jnp
from jax import lax

X = 512
NB = 4
B = 4
STEPS = 1024


def draw_dynamics(key, part):
    first_key, second_key = jax.random.split(key, 2)
    rates = jnp.exp(jax.random.uniform(first_key, (X,), jnp.float32, math.log(1.0 / (2.0 * STEPS)), math.log(1.0 / 30.0)))
    raw_part = jnp.clip(jax.random.normal(second_key, (X, X), jnp.float32), -3.0, 3.0) * (0.035 / math.sqrt(X))
    decay = jnp.exp(-rates)
    skew_part = raw_part - raw_part.T
    return jnp.eye(X, dtype=jnp.float32) * decay[:, None] + skew_part


def draw_obs_index(key, part):
    first_key, second_key = jax.random.split(key, 2)
    base_index = jax.random.randint(first_key, (STEPS,), 0, X, jnp.int32)
    places = jax.random.permutation(second_key, STEPS)[:2]
    base_index = base_index.at[places[0]].set(0)
    return base_index.at[places[1]].set(X - 1)


def place_ends(values, key, least, high):
    longest = values.shape.index(max(values.shape))
    spots = []
    for shift in (0, 1):
        where = [jax.random.randint(jax.random.fold_in(key, axis), (), 0, length) for axis, length in enumerate(values.shape)]
        where[longest] = (where[longest] + shift) % values.shape[longest]
        spots.append(tuple(where))
    return values.at[spots[0]].set(least).at[spots[1]].set(high)


def level_of(key, shape, cuts, smallest, high):
    level = 1.0
    for axis_at, shards_of in cuts:
        draws = jax.random.uniform(jax.random.fold_in(jax.random.fold_in(key, 6), axis_at), (shards_of,), jnp.float32, smallest / len(cuts), high / len(cuts))
        level = level * jnp.repeat(jnp.exp(draws), shape[axis_at] // shards_of).reshape((-1,) + (1,) * (len(shape) - 1 - axis_at))
    return level


def noise(rng, extent, width, most, cuts=(), kind=jnp.bfloat16):
    entries = jax.random.normal(rng, extent, jnp.float32) * width
    if len(cuts) > 0:
        entries = level_of(rng, extent, cuts, -0.22, 0.18) * entries
    return jnp.clip(entries, min=-most, max=most).astype(kind)


def setup_inputs(seed: int = 0) -> dict:
    keys = jax.random.split(jax.random.key(seed), 7)
    return {
        "dynamics": draw_dynamics(jax.random.fold_in(keys[6], 71), 0),
        "pattern": place_ends(jax.random.randint(keys[1], (NB, NB), 0, 2), jax.random.fold_in(keys[1], 1), 0, 1).astype(jnp.int32),
        "initial_mean": noise(keys[2], (B, X), 1.0, 6.0, (), jnp.float32),
        "observed": noise(keys[3], (STEPS, B), 1.0, 6.0, ((0, 64),), jnp.float32),
        "obs_index": draw_obs_index(jax.random.fold_in(keys[6], 71), 0),
        "obs_noise": jnp.clip(jnp.exp(math.log(4.0) - 2.0794415 * jax.random.uniform(keys[5], (STEPS,), jnp.float32) ** level_of(keys[5], (STEPS,), ((0, 64),), -0.2, 0.2)), 0.5, 4.0),
    }


def product(left, right):
    return jnp.dot(left, right, precision=lax.Precision.HIGHEST, preferred_element_type=jnp.float32)


def reference(dynamics, pattern, initial_mean, observed, obs_index, obs_noise):
    blocks = pattern.shape[0]
    state_width = dynamics.shape[0]
    block_span = state_width // blocks
    present = jnp.maximum(pattern, jnp.eye(blocks, dtype=jnp.int32))
    block_mask = jnp.repeat(jnp.repeat(present, block_span, 0), block_span, 1).astype(jnp.float32)
    transition = dynamics * block_mask
    kalman_gains = 1.0 / (1.0 + obs_noise)
    state_index = jnp.arange(state_width, dtype=jnp.int32)
    observed_masks = (state_index[None, :] == obs_index[:, None]).astype(jnp.float32)
    scale_factors = 1.0 - kalman_gains[:, None] * observed_masks

    def filter_update(mean_now, inputs):
        scaling, hit_mask, gain_now, obs_now = inputs
        mean_now = product(mean_now, transition.T) * scaling[None, :] + gain_now * obs_now[:, None] * hit_mask[None, :]
        return mean_now, mean_now

    unused_value, filtered = lax.scan(filter_update, initial_mean, (scale_factors, observed_masks, kalman_gains, observed))
    retain_flags = jnp.ones((STEPS,), jnp.float32).at[STEPS - 1].set(0.0)

    def smoother_update(carried, inputs):
        mean_now, scaling, keep_flag = inputs
        gap_term = mean_now - keep_flag * product(product(mean_now, transition.T), transition) * scaling[None, :]
        carried = keep_flag * product(carried, transition) * scaling[None, :] + gap_term
        return carried, carried

    initial_zeros = jnp.zeros(initial_mean.shape, jnp.float32)
    unused_value, smoothed = lax.scan(smoother_update, initial_zeros, (filtered, scale_factors, retain_flags), reverse=True)
    return filtered, smoothed
```

```python
import jax
import jax.numpy as jnp
from jax import lax
from jax.sharding import PartitionSpec as P

AXES = ("tm", "state")


def product(left, right):
    return jnp.dot(left, right, precision=lax.Precision.HIGHEST, preferred_element_type=jnp.float32)


def transposed(left, right):
    return lax.dot_general(
        left,
        right,
        (((1,), (1,)), ((), ())),
        precision=lax.Precision.HIGHEST,
        preferred_element_type=jnp.float32,
    )


def leading(left, right):
    return lax.dot_general(
        left,
        right,
        (((0,), (0,)), ((), ())),
        precision=lax.Precision.HIGHEST,
        preferred_element_type=jnp.float32,
    )


def shifted(block, distance, total):
    route = [(i, i + distance) for i in range(total) if 0 <= i + distance < total]
    return lax.ppermute(block, AXES, route)


def per_device(dynamics, pattern, initial_mean, observed, obs_index, obs_noise):
    state_width = dynamics.shape[1]
    blocks = pattern.shape[0]
    block_span = state_width // blocks
    seq_total = initial_mean.shape[0]
    members = lax.axis_size("state")
    segments = lax.axis_size("tm") * members
    member = lax.axis_index("state")
    segment = lax.axis_index(AXES)
    span = observed.shape[0] // members
    steps_total = span * segments

    present = jnp.maximum(pattern, jnp.eye(blocks, dtype=jnp.int32))
    block_mask = jnp.repeat(jnp.repeat(present, block_span, 0), block_span, 1).astype(jnp.float32)
    transition = lax.all_gather(dynamics, "state", axis=0, tiled=True) * block_mask

    first = member * span
    obs_here = lax.dynamic_slice_in_dim(observed, first, span, 0)
    index_here = lax.dynamic_slice_in_dim(obs_index, first, span, 0)
    noise_here = lax.dynamic_slice_in_dim(obs_noise, first, span, 0)
    gains = 1.0 / (1.0 + noise_here)
    state_index = jnp.arange(state_width, dtype=jnp.int32)
    hits = (state_index[None, :] == index_here[:, None]).astype(jnp.float32)
    scales = 1.0 - gains[:, None] * hits
    global_step = segment * span + jnp.arange(span, dtype=jnp.int32)
    keeps = jnp.where(global_step == steps_total - 1, 0.0, 1.0).astype(jnp.float32)
    pushes = [(gains[j] * obs_here[j])[:, None] * hits[j][None, :] for j in range(span)]

    filt_a = transition * scales[0][:, None]
    filt_b = pushes[0]
    for j in range(1, span):
        filt_a = product(transition, filt_a) * scales[j][:, None]
        filt_b = transposed(filt_b, transition) * scales[j][None, :] + pushes[j]
    last = span - 1
    smooth_q = keeps[last] * (transition.T * scales[last][:, None])
    for j in range(last - 1, -1, -1):
        smooth_q = keeps[j] * (leading(transition, smooth_q) * scales[j][:, None])

    levels = 0
    while 2 ** (levels + 1) < segments:
        levels += 1
    stored_q = []
    for level in range(levels):
        distance = 2**level
        arrived_a, arrived_b = shifted((filt_a, filt_b), distance, segments)
        arrived_q = shifted(smooth_q, -distance, segments)
        usable = segment >= distance
        new_a = product(filt_a, arrived_a)
        new_b = transposed(arrived_b, filt_a) + filt_b
        filt_a = jnp.where(usable, new_a, filt_a)
        filt_b = jnp.where(usable, new_b, filt_b)
        stored_q.append(smooth_q)
        smooth_q = jnp.where(segment + distance < segments, product(smooth_q, arrived_q), smooth_q)
    stored_q.append(smooth_q)

    top = 2**levels
    prefix = transposed(initial_mean, filt_a) + filt_b
    if top < segments:
        arrived = shifted(prefix, top, segments)
        prefix = jnp.where(segment >= top, transposed(arrived, filt_a) + filt_b, prefix)
    entry = jnp.where(segment == 0, initial_mean, shifted(prefix, 1, segments))

    filtered = []
    current = entry
    for j in range(span):
        current = transposed(current, transition) * scales[j][None, :] + pushes[j]
        filtered.append(current)
    filtered = jnp.stack(filtered)
    mapped = product(
        transposed(filtered.reshape(span * seq_total, state_width), transition), transition
    ).reshape(span, seq_total, state_width)
    gaps = filtered - keeps[:, None, None] * mapped * scales[:, None, :]

    offsets = jnp.zeros((seq_total, state_width), jnp.float32)
    for j in range(last, -1, -1):
        offsets = keeps[j] * product(offsets, transition) * scales[j][None, :] + gaps[j]
    for level in range(levels):
        distance = 2**level
        arrived = shifted(offsets, -distance, segments)
        offsets = jnp.where(
            segment + distance < segments, transposed(arrived, stored_q[level]) + offsets, offsets
        )
    if top < segments:
        arrived = shifted(offsets, -top, segments)
        offsets = jnp.where(
            segment + top < segments, transposed(arrived, stored_q[levels]) + offsets, offsets
        )
    current = shifted(offsets, -1, segments)

    smoothed = [None] * span
    for j in range(last, -1, -1):
        current = keeps[j] * product(current, transition) * scales[j][None, :] + gaps[j]
        smoothed[j] = current
    smoothed = jnp.stack(smoothed)

    both = jnp.stack([filtered, smoothed])
    both = lax.all_to_all(both, "state", split_axis=2, concat_axis=1, tiled=True)
    return (both[0], both[1])


def solution(mesh):
    return jax.shard_map(
        per_device,
        mesh=mesh,
        in_specs=(P("state", None), P(), P(), P("tm", None), P("tm"), P("tm")),
        out_specs=(P("tm", "state", None), P("tm", "state", None)),
        check_vma=False,
    )
```

```python
import jax
import jax.numpy as jnp
from jax import lax
from jax.sharding import PartitionSpec as P

AXES = ("tm", "state")


def product(left, right):
    return jnp.dot(left, right, precision=lax.Precision.HIGHEST, preferred_element_type=jnp.float32)


def transposed(left, right):
    return lax.dot_general(
        left,
        right,
        (((1,), (1,)), ((), ())),
        precision=lax.Precision.HIGHEST,
        preferred_element_type=jnp.float32,
    )


def leading(left, right):
    return lax.dot_general(
        left,
        right,
        (((0,), (0,)), ((), ())),
        precision=lax.Precision.HIGHEST,
        preferred_element_type=jnp.float32,
    )


def shifted(block, distance, total):
    route = [(i, i + distance) for i in range(total) if 0 <= i + distance < total]
    return lax.ppermute(block, AXES, route)


def filter_apply(rows, power, left, right, offsets):
    return transposed(rows, power) + transposed(product(rows, right), left) + offsets


def smoother_apply(rows, power, left, right, offsets):
    return product(rows, power) + transposed(product(rows, right), left) + offsets


def per_device(dynamics, pattern, initial_mean, observed, obs_index, obs_noise):
    state_width = dynamics.shape[1]
    blocks = pattern.shape[0]
    block_span = state_width // blocks
    seq_total = initial_mean.shape[0]
    members = lax.axis_size("state")
    segments = lax.axis_size("tm") * members
    member = lax.axis_index("state")
    segment = lax.axis_index(AXES)
    span = observed.shape[0] // members
    steps_total = span * segments
    last = span - 1

    present = jnp.maximum(pattern, jnp.eye(blocks, dtype=jnp.int32))
    block_mask = jnp.repeat(jnp.repeat(present, block_span, 0), block_span, 1).astype(jnp.float32)
    transition = lax.all_gather(dynamics, "state", axis=0, tiled=True) * block_mask

    first = member * span
    obs_here = lax.dynamic_slice_in_dim(observed, first, span, 0)
    index_here = lax.dynamic_slice_in_dim(obs_index, first, span, 0)
    noise_here = lax.dynamic_slice_in_dim(obs_noise, first, span, 0)
    gains = 1.0 / (1.0 + noise_here)
    state_index = jnp.arange(state_width, dtype=jnp.int32)
    hits = (state_index[None, :] == index_here[:, None]).astype(jnp.float32)
    scales = 1.0 - gains[:, None] * hits
    global_step = segment * span + jnp.arange(span, dtype=jnp.int32)
    keeps = jnp.where(global_step == steps_total - 1, 0.0, 1.0).astype(jnp.float32)
    pushes = [(gains[j] * obs_here[j])[:, None] * hits[j][None, :] for j in range(span)]
    column = jnp.arange(span, dtype=jnp.int32)[:, None]

    chain = max(1, segments // 4)
    powers = []
    power = transition
    length = 1
    while length < span:
        power = product(power, power)
        length *= 2
    powers.append(power)
    while len(powers) < chain.bit_length():
        power = product(power, power)
        powers.append(power)

    hit_columns = hits.T
    moved = [hit_columns]
    for _ in range(last):
        moved.append(product(transition, moved[-1]))
    filt_u = jnp.stack([-gains[j] * moved[last - j][:, j] for j in range(span)], axis=1)
    reach = product(hits, transition)
    for m in range(last - 1, -1, -1):
        reach = jnp.where(column > m, product(reach * scales[m][None, :], transition), reach)
    filt_v = reach.T
    filt_b = pushes[0]
    for j in range(1, span):
        filt_b = transposed(filt_b, transition) * scales[j][None, :] + pushes[j]
    value = initial_mean
    for j in range(span):
        value = transposed(value, transition) * scales[j][None, :] + pushes[j]

    moved = [hit_columns]
    for _ in range(last):
        moved.append(leading(transition, moved[-1]))
    smooth_u = jnp.stack([-gains[j] * moved[j][:, j] for j in range(span)], axis=1)
    reach = transposed(hits, transition)
    for m in range(1, span):
        reach = jnp.where(column < m, transposed(reach * scales[m][None, :], transition), reach)
    smooth_v = reach.T

    stored = []
    level = 0
    while 2**level < chain:
        distance = 2**level
        power = powers[level]
        arrived_u, arrived_v, arrived_b, arrived_value = shifted(
            (filt_u, filt_v, filt_b, value), distance, segments
        )
        new_value = filter_apply(arrived_value, power, filt_u, filt_v, filt_b)
        value = jnp.where((segment >= distance) & (segment < 2 * distance), new_value, value)
        new_u = jnp.concatenate(
            [product(power, arrived_u) + product(filt_u, leading(filt_v, arrived_u)), filt_u], axis=1
        )
        new_v = jnp.concatenate([arrived_v, leading(power, filt_v)], axis=1)
        filt_b = transposed(arrived_b, power) + transposed(product(arrived_b, filt_v), filt_u) + filt_b
        filt_u, filt_v = new_u, new_v

        stored.append((smooth_u, smooth_v))
        arrived_u, arrived_v = shifted((smooth_u, smooth_v), -distance, segments)
        new_u = jnp.concatenate(
            [leading(power, arrived_u) + product(smooth_u, leading(smooth_v, arrived_u)), smooth_u], axis=1
        )
        new_v = jnp.concatenate([arrived_v, product(power, smooth_v)], axis=1)
        smooth_u, smooth_v = new_u, new_v
        level += 1
    stored.append((smooth_u, smooth_v))
    power = powers[level]

    hops = (segments + chain - 1) // chain - 1
    for hop in range(1, hops + 1):
        arrived_value = shifted(value, chain, segments)
        new_value = filter_apply(arrived_value, power, filt_u, filt_v, filt_b)
        value = jnp.where((segment >= hop * chain) & (segment < (hop + 1) * chain), new_value, value)
    entry = jnp.where(segment == 0, initial_mean, shifted(value, 1, segments))

    filtered = []
    current = entry
    for j in range(span):
        current = transposed(current, transition) * scales[j][None, :] + pushes[j]
        filtered.append(current)
    filtered = jnp.stack(filtered)
    mapped = product(
        transposed(filtered.reshape(span * seq_total, state_width), transition), transition
    ).reshape(span, seq_total, state_width)
    gaps = filtered - keeps[:, None, None] * mapped * scales[:, None, :]

    offsets = jnp.zeros((seq_total, state_width), jnp.float32)
    for j in range(last, -1, -1):
        offsets = keeps[j] * product(offsets, transition) * scales[j][None, :] + gaps[j]
    for level in range(len(stored) - 1):
        distance = 2**level
        left, right = stored[level]
        arrived = shifted(offsets, -distance, segments)
        offsets = jnp.where(
            segment + distance < segments,
            smoother_apply(arrived, powers[level], left, right, offsets),
            offsets,
        )
    left, right = stored[-1]
    for hop in range(1, hops + 1):
        arrived = shifted(offsets, -chain, segments)
        new_offsets = smoother_apply(arrived, power, left, right, offsets)
        band = segments - hop * chain
        offsets = jnp.where((segment >= band - chain) & (segment < band), new_offsets, offsets)
    current = shifted(offsets, -1, segments)

    smoothed = [None] * span
    for j in range(last, -1, -1):
        current = keeps[j] * product(current, transition) * scales[j][None, :] + gaps[j]
        smoothed[j] = current
    smoothed = jnp.stack(smoothed)

    both = jnp.stack([filtered, smoothed])
    both = lax.all_to_all(both, "state", split_axis=2, concat_axis=1, tiled=True)
    return (both[0], both[1])


def solution(mesh):
    return jax.shard_map(
        per_device,
        mesh=mesh,
        in_specs=(P("state", None), P(), P(), P("tm", None), P("tm"), P("tm")),
        out_specs=(P("tm", "state", None), P("tm", "state", None)),
        check_vma=False,
    )
```

```python
import jax
import jax.numpy as jnp
from jax import lax
from jax.sharding import PartitionSpec as P

AXES = ("tm", "state")


def product(left, right):
    return jnp.dot(left, right, precision=lax.Precision.HIGHEST, preferred_element_type=jnp.float32)


def transposed(left, right):
    return lax.dot_general(
        left,
        right,
        (((1,), (1,)), ((), ())),
        precision=lax.Precision.HIGHEST,
        preferred_element_type=jnp.float32,
    )


def leading(left, right):
    return lax.dot_general(
        left,
        right,
        (((0,), (0,)), ((), ())),
        precision=lax.Precision.HIGHEST,
        preferred_element_type=jnp.float32,
    )


def shifted(block, distance, total):
    route = [(i, i + distance) for i in range(total) if 0 <= i + distance < total]
    return lax.ppermute(block, AXES, route)


def filter_apply(rows, power, left, right, offsets):
    return transposed(rows, power) + transposed(product(rows, right), left) + offsets


def smoother_apply(rows, power, left, right, offsets):
    return product(rows, power) + transposed(product(rows, right), left) + offsets


def per_device(dynamics, pattern, initial_mean, observed, obs_index, obs_noise):
    state_width = dynamics.shape[1]
    blocks = pattern.shape[0]
    block_span = state_width // blocks
    seq_total = initial_mean.shape[0]
    members = lax.axis_size("state")
    segments = lax.axis_size("tm") * members
    member = lax.axis_index("state")
    segment = lax.axis_index(AXES)
    span = observed.shape[0] // members
    steps_total = span * segments
    last = span - 1

    present = jnp.maximum(pattern, jnp.eye(blocks, dtype=jnp.int32))
    block_mask = jnp.repeat(jnp.repeat(present, block_span, 0), block_span, 1).astype(jnp.float32)
    transition = lax.all_gather(dynamics, "state", axis=0, tiled=True) * block_mask

    first = member * span
    obs_here = lax.dynamic_slice_in_dim(observed, first, span, 0)
    index_here = lax.dynamic_slice_in_dim(obs_index, first, span, 0)
    noise_here = lax.dynamic_slice_in_dim(obs_noise, first, span, 0)
    gains = 1.0 / (1.0 + noise_here)
    state_index = jnp.arange(state_width, dtype=jnp.int32)
    hits = (state_index[None, :] == index_here[:, None]).astype(jnp.float32)
    scales = 1.0 - gains[:, None] * hits
    global_step = segment * span + jnp.arange(span, dtype=jnp.int32)
    keeps = jnp.where(global_step == steps_total - 1, 0.0, 1.0).astype(jnp.float32)
    pushes = [(gains[j] * obs_here[j])[:, None] * hits[j][None, :] for j in range(span)]
    column = jnp.arange(span, dtype=jnp.int32)[:, None]

    chain = max(1, segments // 4)
    powers = []
    power = transition
    length = 1
    while length < span:
        power = product(power, power)
        length *= 2
    powers.append(power)
    while len(powers) < chain.bit_length():
        power = product(power, power)
        powers.append(power)

    hit_columns = hits.T
    moved = [hit_columns]
    for _ in range(last):
        moved.append(product(transition, moved[-1]))
    filt_u = jnp.stack([-gains[j] * moved[last - j][:, j] for j in range(span)], axis=1)
    reach = product(hits, transition)
    for m in range(last - 1, -1, -1):
        reach = jnp.where(column > m, product(reach * scales[m][None, :], transition), reach)
    filt_v = reach.T
    filt_b = pushes[0]
    for j in range(1, span):
        filt_b = transposed(filt_b, transition) * scales[j][None, :] + pushes[j]
    value = initial_mean
    for j in range(span):
        value = transposed(value, transition) * scales[j][None, :] + pushes[j]

    moved = [hit_columns]
    for _ in range(last):
        moved.append(leading(transition, moved[-1]))
    smooth_u = jnp.stack([-gains[j] * moved[j][:, j] for j in range(span)], axis=1)
    reach = transposed(hits, transition)
    for m in range(1, span):
        reach = jnp.where(column < m, transposed(reach * scales[m][None, :], transition), reach)
    smooth_v = reach.T

    stored = []
    level = 0
    while 2**level < chain:
        distance = 2**level
        power = powers[level]
        rank = filt_u.shape[1]
        packed = jnp.concatenate([filt_u, filt_v, filt_b.T, value.T], axis=1)
        packed = shifted(packed, distance, segments)
        arrived_u = packed[:, :rank]
        arrived_v = packed[:, rank : 2 * rank]
        arrived_b = packed[:, 2 * rank : 2 * rank + seq_total].T
        arrived_value = packed[:, 2 * rank + seq_total :].T
        new_value = filter_apply(arrived_value, power, filt_u, filt_v, filt_b)
        value = jnp.where((segment >= distance) & (segment < 2 * distance), new_value, value)
        new_u = jnp.concatenate(
            [product(power, arrived_u) + product(filt_u, leading(filt_v, arrived_u)), filt_u], axis=1
        )
        new_v = jnp.concatenate([arrived_v, leading(power, filt_v)], axis=1)
        filt_b = transposed(arrived_b, power) + transposed(product(arrived_b, filt_v), filt_u) + filt_b
        filt_u, filt_v = new_u, new_v

        stored.append((smooth_u, smooth_v))
        packed = shifted(jnp.concatenate([smooth_u, smooth_v], axis=1), -distance, segments)
        arrived_u = packed[:, :rank]
        arrived_v = packed[:, rank:]
        new_u = jnp.concatenate(
            [leading(power, arrived_u) + product(smooth_u, leading(smooth_v, arrived_u)), smooth_u], axis=1
        )
        new_v = jnp.concatenate([arrived_v, product(power, smooth_v)], axis=1)
        smooth_u, smooth_v = new_u, new_v
        level += 1
    stored.append((smooth_u, smooth_v))
    power = powers[level]

    hops = (segments + chain - 1) // chain - 1
    for hop in range(1, hops + 1):
        arrived_value = shifted(value, chain, segments)
        new_value = filter_apply(arrived_value, power, filt_u, filt_v, filt_b)
        value = jnp.where((segment >= hop * chain) & (segment < (hop + 1) * chain), new_value, value)
    entry = jnp.where(segment == 0, initial_mean, shifted(value, 1, segments))

    filtered = []
    current = entry
    for j in range(span):
        current = transposed(current, transition) * scales[j][None, :] + pushes[j]
        filtered.append(current)
    filtered = jnp.stack(filtered)
    mapped = product(
        transposed(filtered.reshape(span * seq_total, state_width), transition), transition
    ).reshape(span, seq_total, state_width)
    gaps = filtered - keeps[:, None, None] * mapped * scales[:, None, :]

    offsets = jnp.zeros((seq_total, state_width), jnp.float32)
    for j in range(last, -1, -1):
        offsets = keeps[j] * product(offsets, transition) * scales[j][None, :] + gaps[j]
    for level in range(len(stored) - 1):
        distance = 2**level
        left, right = stored[level]
        arrived = shifted(offsets, -distance, segments)
        offsets = jnp.where(
            segment + distance < segments,
            smoother_apply(arrived, powers[level], left, right, offsets),
            offsets,
        )
    left, right = stored[-1]
    for hop in range(1, hops + 1):
        arrived = shifted(offsets, -chain, segments)
        new_offsets = smoother_apply(arrived, power, left, right, offsets)
        band = segments - hop * chain
        offsets = jnp.where((segment >= band - chain) & (segment < band), new_offsets, offsets)
    current = shifted(offsets, -1, segments)

    smoothed = [None] * span
    for j in range(last, -1, -1):
        current = keeps[j] * product(current, transition) * scales[j][None, :] + gaps[j]
        smoothed[j] = current
    smoothed = jnp.stack(smoothed)

    both = jnp.stack([filtered, smoothed])
    both = lax.all_to_all(both, "state", split_axis=2, concat_axis=1, tiled=True)
    return (both[0], both[1])


def solution(mesh):
    return jax.shard_map(
        per_device,
        mesh=mesh,
        in_specs=(P("state", None), P(), P(), P("tm", None), P("tm"), P("tm")),
        out_specs=(P("tm", "state", None), P("tm", "state", None)),
        check_vma=False,
    )
```

```python
import jax
import jax.numpy as jnp
from jax import lax
from jax.sharding import PartitionSpec as P

AXES = ("tm", "state")


def product(left, right):
    return jnp.dot(left, right, precision=lax.Precision.HIGHEST, preferred_element_type=jnp.float32)


def transposed(left, right):
    return lax.dot_general(
        left,
        right,
        (((1,), (1,)), ((), ())),
        precision=lax.Precision.HIGHEST,
        preferred_element_type=jnp.float32,
    )


def leading(left, right):
    return lax.dot_general(
        left,
        right,
        (((0,), (0,)), ((), ())),
        precision=lax.Precision.HIGHEST,
        preferred_element_type=jnp.float32,
    )


def shifted(block, distance, total):
    route = [(i, i + distance) for i in range(total) if 0 <= i + distance < total]
    return lax.ppermute(block, AXES, route)


def filter_apply(rows, power, left, right, offsets):
    return transposed(rows, power) + product(transposed(rows, right), left) + offsets


def smoother_apply(rows, power, left, right, offsets):
    return product(rows, power) + product(transposed(rows, right), left) + offsets


def per_device(dynamics, pattern, initial_mean, observed, obs_index, obs_noise):
    state_width = dynamics.shape[1]
    blocks = pattern.shape[0]
    block_span = state_width // blocks
    seq_total = initial_mean.shape[0]
    members = lax.axis_size("state")
    segments = lax.axis_size("tm") * members
    member = lax.axis_index("state")
    segment = lax.axis_index(AXES)
    span = observed.shape[0] // members
    steps_total = span * segments
    last = span - 1

    present = jnp.maximum(pattern, jnp.eye(blocks, dtype=jnp.int32))
    block_mask = jnp.repeat(jnp.repeat(present, block_span, 0), block_span, 1).astype(jnp.float32)
    transition = lax.all_gather(dynamics, "state", axis=0, tiled=True) * block_mask

    first = member * span
    obs_here = lax.dynamic_slice_in_dim(observed, first, span, 0)
    index_here = lax.dynamic_slice_in_dim(obs_index, first, span, 0)
    noise_here = lax.dynamic_slice_in_dim(obs_noise, first, span, 0)
    gains = 1.0 / (1.0 + noise_here)
    state_index = jnp.arange(state_width, dtype=jnp.int32)
    hits = (state_index[None, :] == index_here[:, None]).astype(jnp.float32)
    scales = 1.0 - gains[:, None] * hits
    global_step = segment * span + jnp.arange(span, dtype=jnp.int32)
    keeps = jnp.where(global_step == steps_total - 1, 0.0, 1.0).astype(jnp.float32)
    pushes = [(gains[j] * obs_here[j])[:, None] * hits[j][None, :] for j in range(span)]
    column = jnp.arange(span, dtype=jnp.int32)[:, None]

    chain = max(1, segments // 4)
    powers = []
    power = transition
    length = 1
    while length < span:
        power = product(power, power)
        length *= 2
    powers.append(power)
    while len(powers) < chain.bit_length():
        power = product(power, power)
        powers.append(power)

    hit_columns = hits.T
    moved = [hit_columns]
    for _ in range(last):
        moved.append(product(transition, moved[-1]))
    filt_u = jnp.stack([-gains[j] * moved[last - j][:, j] for j in range(span)], axis=0)
    reach = product(hits, transition)
    for m in range(last - 1, -1, -1):
        reach = jnp.where(column > m, product(reach * scales[m][None, :], transition), reach)
    filt_v = reach
    filt_b = pushes[0]
    for j in range(1, span):
        filt_b = transposed(filt_b, transition) * scales[j][None, :] + pushes[j]
    value = initial_mean
    for j in range(span):
        value = transposed(value, transition) * scales[j][None, :] + pushes[j]

    moved = [hit_columns]
    for _ in range(last):
        moved.append(leading(transition, moved[-1]))
    smooth_u = jnp.stack([-gains[j] * moved[j][:, j] for j in range(span)], axis=0)
    reach = transposed(hits, transition)
    for m in range(1, span):
        reach = jnp.where(column < m, transposed(reach * scales[m][None, :], transition), reach)
    smooth_v = reach

    stored = []
    level = 0
    while 2**level < chain:
        distance = 2**level
        power = powers[level]
        rank = filt_u.shape[0]
        packed = jnp.concatenate([filt_u, filt_v, filt_b, value], axis=0)
        packed = shifted(packed, distance, segments)
        arrived_u = packed[:rank]
        arrived_v = packed[rank : 2 * rank]
        arrived_b = packed[2 * rank : 2 * rank + seq_total]
        arrived_value = packed[2 * rank + seq_total :]
        new_value = filter_apply(arrived_value, power, filt_u, filt_v, filt_b)
        value = jnp.where((segment >= distance) & (segment < 2 * distance), new_value, value)
        new_u = jnp.concatenate(
            [transposed(arrived_u, power) + product(transposed(arrived_u, filt_v), filt_u), filt_u], axis=0
        )
        new_v = jnp.concatenate([arrived_v, product(filt_v, power)], axis=0)
        filt_b = filter_apply(arrived_b, power, filt_u, filt_v, filt_b)
        filt_u, filt_v = new_u, new_v

        stored.append((smooth_u, smooth_v))
        packed = shifted(jnp.concatenate([smooth_u, smooth_v], axis=0), -distance, segments)
        arrived_u = packed[:rank]
        arrived_v = packed[rank:]
        new_u = jnp.concatenate(
            [product(arrived_u, power) + product(transposed(arrived_u, smooth_v), smooth_u), smooth_u], axis=0
        )
        new_v = jnp.concatenate([arrived_v, transposed(smooth_v, power)], axis=0)
        smooth_u, smooth_v = new_u, new_v
        level += 1
    stored.append((smooth_u, smooth_v))
    power = powers[level]

    hops = (segments + chain - 1) // chain - 1
    for hop in range(1, hops + 1):
        arrived_value = shifted(value, chain, segments)
        new_value = filter_apply(arrived_value, power, filt_u, filt_v, filt_b)
        value = jnp.where((segment >= hop * chain) & (segment < (hop + 1) * chain), new_value, value)
    entry = jnp.where(segment == 0, initial_mean, shifted(value, 1, segments))

    filtered = []
    current = entry
    for j in range(span):
        current = transposed(current, transition) * scales[j][None, :] + pushes[j]
        filtered.append(current)
    filtered = jnp.stack(filtered)
    mapped = product(
        transposed(filtered.reshape(span * seq_total, state_width), transition), transition
    ).reshape(span, seq_total, state_width)
    gaps = filtered - keeps[:, None, None] * mapped * scales[:, None, :]

    offsets = jnp.zeros((seq_total, state_width), jnp.float32)
    for j in range(last, -1, -1):
        offsets = keeps[j] * product(offsets, transition) * scales[j][None, :] + gaps[j]
    for level in range(len(stored) - 1):
        distance = 2**level
        left, right = stored[level]
        arrived = shifted(offsets, -distance, segments)
        offsets = jnp.where(
            segment + distance < segments,
            smoother_apply(arrived, powers[level], left, right, offsets),
            offsets,
        )
    left, right = stored[-1]
    for hop in range(1, hops + 1):
        arrived = shifted(offsets, -chain, segments)
        new_offsets = smoother_apply(arrived, power, left, right, offsets)
        band = segments - hop * chain
        offsets = jnp.where((segment >= band - chain) & (segment < band), new_offsets, offsets)
    current = shifted(offsets, -1, segments)

    smoothed = [None] * span
    for j in range(last, -1, -1):
        current = keeps[j] * product(current, transition) * scales[j][None, :] + gaps[j]
        smoothed[j] = current
    smoothed = jnp.stack(smoothed)

    both = jnp.stack([filtered, smoothed])
    both = lax.all_to_all(both, "state", split_axis=2, concat_axis=1, tiled=True)
    return (both[0], both[1])


def solution(mesh):
    return jax.shard_map(
        per_device,
        mesh=mesh,
        in_specs=(P("state", None), P(), P(), P("tm", None), P("tm"), P("tm")),
        out_specs=(P("tm", "state", None), P("tm", "state", None)),
        check_vma=False,
    )
```

```python
import jax
import jax.numpy as jnp
from jax import lax
from jax.sharding import PartitionSpec as P

AXES = ("tm", "state")


def product(left, right):
    return jnp.dot(left, right, precision=lax.Precision.HIGHEST, preferred_element_type=jnp.float32)


def transposed(left, right):
    return lax.dot_general(
        left,
        right,
        (((1,), (1,)), ((), ())),
        precision=lax.Precision.HIGHEST,
        preferred_element_type=jnp.float32,
    )


def leading(left, right):
    return lax.dot_general(
        left,
        right,
        (((0,), (0,)), ((), ())),
        precision=lax.Precision.HIGHEST,
        preferred_element_type=jnp.float32,
    )


def shifted(block, distance, total):
    route = [(i, i + distance) for i in range(total) if 0 <= i + distance < total]
    return lax.ppermute(block, AXES, route)


def filter_apply(rows, power, left, right, offsets):
    return transposed(rows, power) + product(transposed(rows, right), left) + offsets


def smoother_apply(rows, power, left, right, offsets):
    return product(rows, power) + product(transposed(rows, right), left) + offsets


def per_device(dynamics, pattern, initial_mean, observed, obs_index, obs_noise):
    state_width = dynamics.shape[1]
    blocks = pattern.shape[0]
    block_span = state_width // blocks
    seq_total = initial_mean.shape[0]
    members = lax.axis_size("state")
    segments = lax.axis_size("tm") * members
    member = lax.axis_index("state")
    segment = lax.axis_index(AXES)
    span = observed.shape[0] // members
    steps_total = span * segments
    last = span - 1

    present = jnp.maximum(pattern, jnp.eye(blocks, dtype=jnp.int32))
    block_mask = jnp.repeat(jnp.repeat(present, block_span, 0), block_span, 1).astype(jnp.float32)
    pieces = [dynamics]
    for step in range(1, members):
        route = [(i, (i + step) % members) for i in range(members)]
        pieces.append(lax.ppermute(dynamics, "state", route))
    order = (member - jnp.arange(members, dtype=jnp.int32)) % members
    gathered = jnp.take(jnp.stack(pieces), order, axis=0).reshape(state_width, state_width)
    transition = gathered * block_mask

    first = member * span
    obs_here = lax.dynamic_slice_in_dim(observed, first, span, 0)
    index_here = lax.dynamic_slice_in_dim(obs_index, first, span, 0)
    noise_here = lax.dynamic_slice_in_dim(obs_noise, first, span, 0)
    gains = 1.0 / (1.0 + noise_here)
    state_index = jnp.arange(state_width, dtype=jnp.int32)
    hits = (state_index[None, :] == index_here[:, None]).astype(jnp.float32)
    scales = 1.0 - gains[:, None] * hits
    global_step = segment * span + jnp.arange(span, dtype=jnp.int32)
    keeps = jnp.where(global_step == steps_total - 1, 0.0, 1.0).astype(jnp.float32)
    pushes = [(gains[j] * obs_here[j])[:, None] * hits[j][None, :] for j in range(span)]
    column = jnp.arange(span, dtype=jnp.int32)[:, None]

    chain = max(1, segments // 4)
    powers = []
    power = transition
    length = 1
    while length < span:
        power = product(power, power)
        length *= 2
    powers.append(power)
    while len(powers) < chain.bit_length():
        power = product(power, power)
        powers.append(power)

    hit_columns = hits.T
    moved = [hit_columns]
    for _ in range(last):
        moved.append(product(transition, moved[-1]))
    filt_u = jnp.stack([-gains[j] * moved[last - j][:, j] for j in range(span)], axis=0)
    reach = product(hits, transition)
    for m in range(last - 1, -1, -1):
        reach = jnp.where(column > m, product(reach * scales[m][None, :], transition), reach)
    filt_v = reach
    filt_b = pushes[0]
    for j in range(1, span):
        filt_b = transposed(filt_b, transition) * scales[j][None, :] + pushes[j]
    value = initial_mean
    for j in range(span):
        value = transposed(value, transition) * scales[j][None, :] + pushes[j]

    moved = [hit_columns]
    for _ in range(last):
        moved.append(leading(transition, moved[-1]))
    smooth_u = jnp.stack([-gains[j] * moved[j][:, j] for j in range(span)], axis=0)
    reach = transposed(hits, transition)
    for m in range(1, span):
        reach = jnp.where(column < m, transposed(reach * scales[m][None, :], transition), reach)
    smooth_v = reach

    stored = []
    level = 0
    while 2**level < chain:
        distance = 2**level
        power = powers[level]
        rank = filt_u.shape[0]
        packed = jnp.concatenate([filt_u, filt_v, filt_b, value], axis=0)
        packed = shifted(packed, distance, segments)
        arrived_u = packed[:rank]
        arrived_v = packed[rank : 2 * rank]
        arrived_b = packed[2 * rank : 2 * rank + seq_total]
        arrived_value = packed[2 * rank + seq_total :]
        new_value = filter_apply(arrived_value, power, filt_u, filt_v, filt_b)
        value = jnp.where((segment >= distance) & (segment < 2 * distance), new_value, value)
        new_u = jnp.concatenate(
            [transposed(arrived_u, power) + product(transposed(arrived_u, filt_v), filt_u), filt_u], axis=0
        )
        new_v = jnp.concatenate([arrived_v, product(filt_v, power)], axis=0)
        filt_b = filter_apply(arrived_b, power, filt_u, filt_v, filt_b)
        filt_u, filt_v, filt_b = lax.optimization_barrier((new_u, new_v, filt_b))

        stored.append((smooth_u, smooth_v))
        packed = shifted(jnp.concatenate([smooth_u, smooth_v], axis=0), -distance, segments)
        arrived_u = packed[:rank]
        arrived_v = packed[rank:]
        new_u = jnp.concatenate(
            [product(arrived_u, power) + product(transposed(arrived_u, smooth_v), smooth_u), smooth_u], axis=0
        )
        new_v = jnp.concatenate([arrived_v, transposed(smooth_v, power)], axis=0)
        smooth_u, smooth_v = lax.optimization_barrier((new_u, new_v))
        level += 1
    stored.append((smooth_u, smooth_v))
    power = powers[level]

    hops = (segments + chain - 1) // chain - 1
    for hop in range(1, hops + 1):
        arrived_value = shifted(value, chain, segments)
        new_value = filter_apply(arrived_value, power, filt_u, filt_v, filt_b)
        value = jnp.where((segment >= hop * chain) & (segment < (hop + 1) * chain), new_value, value)
    entry = jnp.where(segment == 0, initial_mean, shifted(value, 1, segments))

    filtered = []
    current = entry
    for j in range(span):
        current = transposed(current, transition) * scales[j][None, :] + pushes[j]
        filtered.append(current)
    filtered = jnp.stack(filtered)
    mapped = product(
        transposed(filtered.reshape(span * seq_total, state_width), transition), transition
    ).reshape(span, seq_total, state_width)
    gaps = filtered - keeps[:, None, None] * mapped * scales[:, None, :]

    offsets = jnp.zeros((seq_total, state_width), jnp.float32)
    for j in range(last, -1, -1):
        offsets = keeps[j] * product(offsets, transition) * scales[j][None, :] + gaps[j]
    for level in range(len(stored) - 1):
        distance = 2**level
        left, right = stored[level]
        arrived = shifted(offsets, -distance, segments)
        offsets = jnp.where(
            segment + distance < segments,
            smoother_apply(arrived, powers[level], left, right, offsets),
            offsets,
        )
    left, right = stored[-1]
    for hop in range(1, hops + 1):
        arrived = shifted(offsets, -chain, segments)
        new_offsets = smoother_apply(arrived, power, left, right, offsets)
        band = segments - hop * chain
        offsets = jnp.where((segment >= band - chain) & (segment < band), new_offsets, offsets)
    current = shifted(offsets, -1, segments)

    smoothed = [None] * span
    for j in range(last, -1, -1):
        current = keeps[j] * product(current, transition) * scales[j][None, :] + gaps[j]
        smoothed[j] = current
    smoothed = jnp.stack(smoothed)

    both = jnp.stack([filtered, smoothed])
    both = lax.all_to_all(both, "state", split_axis=2, concat_axis=1, tiled=True)
    return (both[0], both[1])


def solution(mesh):
    return jax.shard_map(
        per_device,
        mesh=mesh,
        in_specs=(P("state", None), P(), P(), P("tm", None), P("tm"), P("tm")),
        out_specs=(P("tm", "state", None), P("tm", "state", None)),
        check_vma=False,
    )
```

```python
import jax
import jax.numpy as jnp
from jax import lax
from jax.sharding import PartitionSpec as P

AXES = ("tm", "state")


def product(left, right):
    return jnp.dot(left, right, precision=lax.Precision.HIGHEST, preferred_element_type=jnp.float32)


def transposed(left, right):
    return lax.dot_general(
        left,
        right,
        (((1,), (1,)), ((), ())),
        precision=lax.Precision.HIGHEST,
        preferred_element_type=jnp.float32,
    )


def leading(left, right):
    return lax.dot_general(
        left,
        right,
        (((0,), (0,)), ((), ())),
        precision=lax.Precision.HIGHEST,
        preferred_element_type=jnp.float32,
    )


PLACEMENTS = {256: (4, 1, 7, 6, 0, 2, 3, 5), 16: (2, 0, 3, 1)}


def placement(total):
    bits = PLACEMENTS.get(total)
    if bits is None:
        return list(range(total))
    order = []
    for seg in range(total):
        device = 0
        for place, bit in enumerate(bits):
            device |= ((seg >> place) & 1) << bit
        order.append(device)
    return order


def shifted(block, distance, total):
    order = placement(total)
    route = [(order[i], order[i + distance]) for i in range(total) if 0 <= i + distance < total]
    return lax.ppermute(block, AXES, route)


def filter_apply(rows, power, left, right, offsets):
    return transposed(rows, power) + product(transposed(rows, right), left) + offsets


def smoother_apply(rows, power, left, right, offsets):
    return product(rows, power) + product(transposed(rows, right), left) + offsets


def per_device(dynamics, pattern, initial_mean, observed, obs_index, obs_noise):
    state_width = dynamics.shape[1]
    blocks = pattern.shape[0]
    block_span = state_width // blocks
    seq_total = initial_mean.shape[0]
    members = lax.axis_size("state")
    segments = lax.axis_size("tm") * members
    member = lax.axis_index("state")
    order = placement(segments)
    owner = [0] * segments
    for seg, device in enumerate(order):
        owner[device] = seg
    segment = jnp.asarray(owner, jnp.int32)[lax.axis_index(AXES)]
    span = observed.shape[0] // members
    steps_total = span * segments
    last = span - 1

    present = jnp.maximum(pattern, jnp.eye(blocks, dtype=jnp.int32))
    block_mask = jnp.repeat(jnp.repeat(present, block_span, 0), block_span, 1).astype(jnp.float32)
    pieces = [dynamics]
    for step in range(1, members):
        route = [(i, (i + step) % members) for i in range(members)]
        pieces.append(lax.ppermute(dynamics, "state", route))
    sources = (member - jnp.arange(members, dtype=jnp.int32)) % members
    gathered = jnp.take(jnp.stack(pieces), sources, axis=0).reshape(state_width, state_width)
    transition = gathered * block_mask

    first = member * span
    obs_here = lax.dynamic_slice_in_dim(observed, first, span, 0)
    index_here = lax.dynamic_slice_in_dim(obs_index, first, span, 0)
    noise_here = lax.dynamic_slice_in_dim(obs_noise, first, span, 0)
    route = [(seg, order[seg]) for seg in range(segments)]
    floats = lax.ppermute(jnp.concatenate([obs_here, noise_here[:, None]], axis=1), AXES, route)
    index_here = lax.ppermute(index_here, AXES, route)
    obs_here = floats[:, :seq_total]
    noise_here = floats[:, seq_total]
    gains = 1.0 / (1.0 + noise_here)
    state_index = jnp.arange(state_width, dtype=jnp.int32)
    hits = (state_index[None, :] == index_here[:, None]).astype(jnp.float32)
    scales = 1.0 - gains[:, None] * hits
    global_step = segment * span + jnp.arange(span, dtype=jnp.int32)
    keeps = jnp.where(global_step == steps_total - 1, 0.0, 1.0).astype(jnp.float32)
    pushes = [(gains[j] * obs_here[j])[:, None] * hits[j][None, :] for j in range(span)]
    column = jnp.arange(span, dtype=jnp.int32)[:, None]

    chain = max(1, segments // 4)
    powers = []
    power = transition
    length = 1
    while length < span:
        power = product(power, power)
        length *= 2
    powers.append(power)
    while len(powers) < chain.bit_length():
        power = product(power, power)
        powers.append(power)

    hit_columns = hits.T
    moved = [hit_columns]
    for _ in range(last):
        moved.append(product(transition, moved[-1]))
    filt_u = jnp.stack([-gains[j] * moved[last - j][:, j] for j in range(span)], axis=0)
    reach = product(hits, transition)
    for m in range(last - 1, -1, -1):
        reach = jnp.where(column > m, product(reach * scales[m][None, :], transition), reach)
    filt_v = reach
    filt_b = pushes[0]
    for j in range(1, span):
        filt_b = transposed(filt_b, transition) * scales[j][None, :] + pushes[j]
    value = initial_mean
    for j in range(span):
        value = transposed(value, transition) * scales[j][None, :] + pushes[j]

    moved = [hit_columns]
    for _ in range(last):
        moved.append(leading(transition, moved[-1]))
    smooth_u = jnp.stack([-gains[j] * moved[j][:, j] for j in range(span)], axis=0)
    reach = transposed(hits, transition)
    for m in range(1, span):
        reach = jnp.where(column < m, transposed(reach * scales[m][None, :], transition), reach)
    smooth_v = reach

    stored = []
    level = 0
    while 2**level < chain:
        distance = 2**level
        power = powers[level]
        rank = filt_u.shape[0]
        packed = jnp.concatenate([filt_u, filt_v, filt_b, value], axis=0)
        packed = shifted(packed, distance, segments)
        arrived_u = packed[:rank]
        arrived_v = packed[rank : 2 * rank]
        arrived_b = packed[2 * rank : 2 * rank + seq_total]
        arrived_value = packed[2 * rank + seq_total :]
        new_value = filter_apply(arrived_value, power, filt_u, filt_v, filt_b)
        value = jnp.where((segment >= distance) & (segment < 2 * distance), new_value, value)
        new_u = jnp.concatenate(
            [transposed(arrived_u, power) + product(transposed(arrived_u, filt_v), filt_u), filt_u], axis=0
        )
        new_v = jnp.concatenate([arrived_v, product(filt_v, power)], axis=0)
        filt_b = filter_apply(arrived_b, power, filt_u, filt_v, filt_b)
        filt_u, filt_v, filt_b = lax.optimization_barrier((new_u, new_v, filt_b))

        stored.append((smooth_u, smooth_v))
        packed = shifted(jnp.concatenate([smooth_u, smooth_v], axis=0), -distance, segments)
        arrived_u = packed[:rank]
        arrived_v = packed[rank:]
        new_u = jnp.concatenate(
            [product(arrived_u, power) + product(transposed(arrived_u, smooth_v), smooth_u), smooth_u], axis=0
        )
        new_v = jnp.concatenate([arrived_v, transposed(smooth_v, power)], axis=0)
        smooth_u, smooth_v = lax.optimization_barrier((new_u, new_v))
        level += 1
    stored.append((smooth_u, smooth_v))
    power = powers[level]

    hops = (segments + chain - 1) // chain - 1
    for hop in range(1, hops + 1):
        arrived_value = shifted(value, chain, segments)
        new_value = filter_apply(arrived_value, power, filt_u, filt_v, filt_b)
        value = jnp.where((segment >= hop * chain) & (segment < (hop + 1) * chain), new_value, value)
    entry = jnp.where(segment == 0, initial_mean, shifted(value, 1, segments))

    filtered = []
    current = entry
    for j in range(span):
        current = transposed(current, transition) * scales[j][None, :] + pushes[j]
        filtered.append(current)
    filtered = jnp.stack(filtered)
    mapped = product(
        transposed(filtered.reshape(span * seq_total, state_width), transition), transition
    ).reshape(span, seq_total, state_width)
    gaps = filtered - keeps[:, None, None] * mapped * scales[:, None, :]

    offsets = jnp.zeros((seq_total, state_width), jnp.float32)
    for j in range(last, -1, -1):
        offsets = keeps[j] * product(offsets, transition) * scales[j][None, :] + gaps[j]
    for level in range(len(stored) - 1):
        distance = 2**level
        left, right = stored[level]
        arrived = shifted(offsets, -distance, segments)
        offsets = jnp.where(
            segment + distance < segments,
            smoother_apply(arrived, powers[level], left, right, offsets),
            offsets,
        )
    left, right = stored[-1]
    for hop in range(1, hops + 1):
        arrived = shifted(offsets, -chain, segments)
        new_offsets = smoother_apply(arrived, power, left, right, offsets)
        band = segments - hop * chain
        offsets = jnp.where((segment >= band - chain) & (segment < band), new_offsets, offsets)
    current = shifted(offsets, -1, segments)

    smoothed = [None] * span
    for j in range(last, -1, -1):
        current = keeps[j] * product(current, transition) * scales[j][None, :] + gaps[j]
        smoothed[j] = current
    smoothed = jnp.stack(smoothed)

    both = jnp.stack([filtered, smoothed])
    received = []
    for turn in range(members):
        piece = lax.dynamic_index_in_dim(both, (segment % members + turn) % members, axis=2, keepdims=False)
        route = [
            (order[seg], (seg // members) * members + (seg % members + turn) % members)
            for seg in range(segments)
        ]
        received.append(lax.ppermute(piece, AXES, route))
    picks = (member - jnp.arange(members, dtype=jnp.int32)) % members
    placed = jnp.take(jnp.stack(received), picks, axis=0)
    placed = jnp.moveaxis(placed, 1, 0).reshape(2, members * span, 1, state_width)
    return (placed[0], placed[1])


def solution(mesh):
    return jax.shard_map(
        per_device,
        mesh=mesh,
        in_specs=(P("state", None), P(), P(), P("tm", None), P("tm"), P("tm")),
        out_specs=(P("tm", "state", None), P("tm", "state", None)),
        check_vma=False,
    )
```

```python
import jax
import jax.numpy as jnp
from jax import lax
from jax.sharding import PartitionSpec as P

AXES = ("tm", "state")


def product(left, right):
    return jnp.dot(left, right, precision=lax.Precision.HIGHEST, preferred_element_type=jnp.float32)


def transposed(left, right):
    return lax.dot_general(
        left,
        right,
        (((1,), (1,)), ((), ())),
        precision=lax.Precision.HIGHEST,
        preferred_element_type=jnp.float32,
    )


def leading(left, right):
    return lax.dot_general(
        left,
        right,
        (((0,), (0,)), ((), ())),
        precision=lax.Precision.HIGHEST,
        preferred_element_type=jnp.float32,
    )


def paired(left, right):
    return lax.dot_general(
        left,
        right,
        (((2,), (1,)), ((0,), (0,))),
        precision=lax.Precision.HIGHEST,
        preferred_element_type=jnp.float32,
    )


def shifted(block, distance, total):
    route = [(i, i + distance) for i in range(total) if 0 <= i + distance < total]
    return lax.ppermute(block, AXES, route)


def filter_apply(rows, power, left, right, offsets):
    return transposed(rows, power) + product(transposed(rows, right), left) + offsets


def smoother_apply(rows, power, left, right, offsets):
    return product(rows, power) + product(transposed(rows, right), left) + offsets


def per_device(dynamics, pattern, initial_mean, observed, obs_index, obs_noise):
    state_width = dynamics.shape[1]
    blocks = pattern.shape[0]
    block_span = state_width // blocks
    seq_total = initial_mean.shape[0]
    members = lax.axis_size("state")
    segments = lax.axis_size("tm") * members
    member = lax.axis_index("state")
    segment = lax.axis_index(AXES)
    span = observed.shape[0] // members
    steps_total = span * segments
    last = span - 1

    present = jnp.maximum(pattern, jnp.eye(blocks, dtype=jnp.int32))
    block_mask = jnp.repeat(jnp.repeat(present, block_span, 0), block_span, 1).astype(jnp.float32)
    pieces = [dynamics]
    for step in range(1, members):
        route = [(i, (i + step) % members) for i in range(members)]
        pieces.append(lax.ppermute(dynamics, "state", route))
    order = (member - jnp.arange(members, dtype=jnp.int32)) % members
    gathered = jnp.take(jnp.stack(pieces), order, axis=0).reshape(state_width, state_width)
    transition = gathered * block_mask

    first = member * span
    obs_here = lax.dynamic_slice_in_dim(observed, first, span, 0)
    index_here = lax.dynamic_slice_in_dim(obs_index, first, span, 0)
    noise_here = lax.dynamic_slice_in_dim(obs_noise, first, span, 0)
    gains = 1.0 / (1.0 + noise_here)
    state_index = jnp.arange(state_width, dtype=jnp.int32)
    hits = (state_index[None, :] == index_here[:, None]).astype(jnp.float32)
    scales = 1.0 - gains[:, None] * hits
    global_step = segment * span + jnp.arange(span, dtype=jnp.int32)
    keeps = jnp.where(global_step == steps_total - 1, 0.0, 1.0).astype(jnp.float32)
    pushes = [(gains[j] * obs_here[j])[:, None] * hits[j][None, :] for j in range(span)]
    column = jnp.arange(span, dtype=jnp.int32)[:, None]

    chain = max(1, segments // 4)
    powers = []
    power = transition
    length = 1
    while length < span:
        power = product(power, power)
        length *= 2
    powers.append(power)
    while len(powers) < chain.bit_length():
        power = product(power, power)
        powers.append(power)

    pair = jnp.stack([transition, transition.T])
    hit_columns = hits.T
    current = jnp.stack([hit_columns, hit_columns])
    moved = [current]
    for _ in range(last):
        current = paired(pair, current)
        moved.append(current)
    filt_u = jnp.stack([-gains[j] * moved[last - j][0, :, j] for j in range(span)], axis=0)
    smooth_u = jnp.stack([-gains[j] * moved[j][1, :, j] for j in range(span)], axis=0)
    reach = paired(jnp.stack([hits, hits]), pair)
    for turn in range(last):
        later, earlier = last - 1 - turn, 1 + turn
        scaled = jnp.stack([reach[0] * scales[later][None, :], reach[1] * scales[earlier][None, :]])
        moved_rows = paired(scaled, pair)
        reach = jnp.stack(
            [
                jnp.where(column > later, moved_rows[0], reach[0]),
                jnp.where(column < earlier, moved_rows[1], reach[1]),
            ]
        )
    filt_v, smooth_v = reach[0], reach[1]
    sweep = jnp.concatenate([jnp.zeros_like(initial_mean), initial_mean], axis=0)
    for j in range(span):
        sweep = transposed(sweep, transition) * scales[j][None, :] + jnp.concatenate([pushes[j], pushes[j]], axis=0)
    filt_b, value = sweep[:seq_total], sweep[seq_total:]

    stored = []
    level = 0
    while 2**level < chain:
        distance = 2**level
        power = powers[level]
        rank = filt_u.shape[0]
        packed = jnp.concatenate([filt_u, filt_v, filt_b, value], axis=0)
        packed = shifted(packed, distance, segments)
        arrived_u = packed[:rank]
        arrived_v = packed[rank : 2 * rank]
        arrived_b = packed[2 * rank : 2 * rank + seq_total]
        arrived_value = packed[2 * rank + seq_total :]
        new_value = filter_apply(arrived_value, power, filt_u, filt_v, filt_b)
        value = jnp.where((segment >= distance) & (segment < 2 * distance), new_value, value)
        new_u = jnp.concatenate(
            [transposed(arrived_u, power) + product(transposed(arrived_u, filt_v), filt_u), filt_u], axis=0
        )
        new_v = jnp.concatenate([arrived_v, product(filt_v, power)], axis=0)
        filt_b = filter_apply(arrived_b, power, filt_u, filt_v, filt_b)
        filt_u, filt_v, filt_b = lax.optimization_barrier((new_u, new_v, filt_b))

        stored.append((smooth_u, smooth_v))
        packed = shifted(jnp.concatenate([smooth_u, smooth_v], axis=0), -distance, segments)
        arrived_u = packed[:rank]
        arrived_v = packed[rank:]
        new_u = jnp.concatenate(
            [product(arrived_u, power) + product(transposed(arrived_u, smooth_v), smooth_u), smooth_u], axis=0
        )
        new_v = jnp.concatenate([arrived_v, transposed(smooth_v, power)], axis=0)
        smooth_u, smooth_v = lax.optimization_barrier((new_u, new_v))
        level += 1
    stored.append((smooth_u, smooth_v))
    power = powers[level]

    hops = (segments + chain - 1) // chain - 1
    for hop in range(1, hops + 1):
        arrived_value = shifted(value, chain, segments)
        new_value = filter_apply(arrived_value, power, filt_u, filt_v, filt_b)
        value = jnp.where((segment >= hop * chain) & (segment < (hop + 1) * chain), new_value, value)
    entry = jnp.where(segment == 0, initial_mean, shifted(value, 1, segments))

    filtered = []
    current = entry
    for j in range(span):
        current = transposed(current, transition) * scales[j][None, :] + pushes[j]
        filtered.append(current)
    filtered = jnp.stack(filtered)
    mapped = product(
        transposed(filtered.reshape(span * seq_total, state_width), transition), transition
    ).reshape(span, seq_total, state_width)
    gaps = filtered - keeps[:, None, None] * mapped * scales[:, None, :]

    offsets = jnp.zeros((seq_total, state_width), jnp.float32)
    for j in range(last, -1, -1):
        offsets = keeps[j] * product(offsets, transition) * scales[j][None, :] + gaps[j]
    for level in range(len(stored) - 1):
        distance = 2**level
        left, right = stored[level]
        arrived = shifted(offsets, -distance, segments)
        offsets = jnp.where(
            segment + distance < segments,
            smoother_apply(arrived, powers[level], left, right, offsets),
            offsets,
        )
    left, right = stored[-1]
    for hop in range(1, hops + 1):
        arrived = shifted(offsets, -chain, segments)
        new_offsets = smoother_apply(arrived, power, left, right, offsets)
        band = segments - hop * chain
        offsets = jnp.where((segment >= band - chain) & (segment < band), new_offsets, offsets)
    current = shifted(offsets, -1, segments)

    smoothed = [None] * span
    for j in range(last, -1, -1):
        current = keeps[j] * product(current, transition) * scales[j][None, :] + gaps[j]
        smoothed[j] = current
    smoothed = jnp.stack(smoothed)

    both = jnp.stack([filtered, smoothed])
    both = lax.all_to_all(both, "state", split_axis=2, concat_axis=1, tiled=True)
    return (both[0], both[1])


def solution(mesh):
    return jax.shard_map(
        per_device,
        mesh=mesh,
        in_specs=(P("state", None), P(), P(), P("tm", None), P("tm"), P("tm")),
        out_specs=(P("tm", "state", None), P("tm", "state", None)),
        check_vma=False,
    )
```

```python
import jax
import jax.numpy as jnp
from jax import lax
from jax.sharding import PartitionSpec as P

AXES = ("tm", "state")


def product(left, right):
    return jnp.dot(left, right, precision=lax.Precision.HIGHEST, preferred_element_type=jnp.float32)


def transposed(left, right):
    return lax.dot_general(
        left,
        right,
        (((1,), (1,)), ((), ())),
        precision=lax.Precision.HIGHEST,
        preferred_element_type=jnp.float32,
    )


def leading(left, right):
    return lax.dot_general(
        left,
        right,
        (((0,), (0,)), ((), ())),
        precision=lax.Precision.HIGHEST,
        preferred_element_type=jnp.float32,
    )


def paired(left, right):
    return lax.dot_general(
        left,
        right,
        (((2,), (1,)), ((0,), (0,))),
        precision=lax.Precision.HIGHEST,
        preferred_element_type=jnp.float32,
    )


def shifted(block, distance, total):
    route = [(i, i + distance) for i in range(total) if 0 <= i + distance < total]
    return lax.ppermute(block, AXES, route)


def filter_apply(rows, power, left, right, offsets):
    return transposed(rows, power) + product(transposed(rows, right), left) + offsets


def smoother_apply(rows, power, left, right, offsets):
    return product(rows, power) + product(transposed(rows, right), left) + offsets


def per_device(dynamics, pattern, initial_mean, observed, obs_index, obs_noise):
    state_width = dynamics.shape[1]
    blocks = pattern.shape[0]
    block_span = state_width // blocks
    seq_total = initial_mean.shape[0]
    members = lax.axis_size("state")
    segments = lax.axis_size("tm") * members
    member = lax.axis_index("state")
    segment = lax.axis_index(AXES)
    span = observed.shape[0] // members
    steps_total = span * segments
    last = span - 1

    present = jnp.maximum(pattern, jnp.eye(blocks, dtype=jnp.int32))
    block_mask = jnp.repeat(jnp.repeat(present, block_span, 0), block_span, 1).astype(jnp.float32)
    pieces = [dynamics]
    for step in range(1, members):
        route = [(i, (i + step) % members) for i in range(members)]
        pieces.append(lax.ppermute(dynamics, "state", route))
    order = (member - jnp.arange(members, dtype=jnp.int32)) % members
    gathered = jnp.take(jnp.stack(pieces), order, axis=0).reshape(state_width, state_width)
    transition = gathered * block_mask

    first = member * span
    obs_here = lax.dynamic_slice_in_dim(observed, first, span, 0)
    index_here = lax.dynamic_slice_in_dim(obs_index, first, span, 0)
    noise_here = lax.dynamic_slice_in_dim(obs_noise, first, span, 0)
    gains = 1.0 / (1.0 + noise_here)
    state_index = jnp.arange(state_width, dtype=jnp.int32)
    hits = (state_index[None, :] == index_here[:, None]).astype(jnp.float32)
    scales = 1.0 - gains[:, None] * hits
    global_step = segment * span + jnp.arange(span, dtype=jnp.int32)
    keeps = jnp.where(global_step == steps_total - 1, 0.0, 1.0).astype(jnp.float32)
    pushes = [(gains[j] * obs_here[j])[:, None] * hits[j][None, :] for j in range(span)]
    column = jnp.arange(span, dtype=jnp.int32)[:, None]

    pair = jnp.stack([transition, transition.T])
    hit_columns = hits.T
    current = jnp.stack([hit_columns, hit_columns])
    moved = [current]
    for _ in range(last):
        current = paired(pair, current)
        moved.append(current)
    filt_u = jnp.stack([-gains[j] * moved[last - j][0, :, j] for j in range(span)], axis=0)
    smooth_u = jnp.stack([-gains[j] * moved[j][1, :, j] for j in range(span)], axis=0)
    reach = paired(jnp.stack([hits, hits]), pair)
    for turn in range(last):
        later, earlier = last - 1 - turn, 1 + turn
        scaled = jnp.stack([reach[0] * scales[later][None, :], reach[1] * scales[earlier][None, :]])
        moved_rows = paired(scaled, pair)
        reach = jnp.stack(
            [
                jnp.where(column > later, moved_rows[0], reach[0]),
                jnp.where(column < earlier, moved_rows[1], reach[1]),
            ]
        )
    filt_v, smooth_v = reach[0], reach[1]
    sweep = jnp.concatenate([jnp.zeros_like(initial_mean), initial_mean], axis=0)
    for j in range(span):
        sweep = transposed(sweep, transition) * scales[j][None, :] + jnp.concatenate([pushes[j], pushes[j]], axis=0)
    filt_b, value = sweep[:seq_total], sweep[seq_total:]

    first_filter = jnp.concatenate([filt_u, filt_v, filt_b, value], axis=0)
    first_smoother = jnp.concatenate([smooth_u, smooth_v], axis=0)
    first_filter, first_smoother, base = lax.optimization_barrier((first_filter, first_smoother, transition))
    chain = max(1, segments // 4)
    powers = []
    power = base
    length = 1
    while length < span:
        power = product(power, power)
        length *= 2
    powers.append(power)
    while len(powers) < chain.bit_length():
        power = product(power, power)
        powers.append(power)

    stored = []
    level = 0
    while 2**level < chain:
        distance = 2**level
        power = powers[level]
        rank = filt_u.shape[0]
        if level == 0:
            packed = first_filter
        else:
            packed = jnp.concatenate([filt_u, filt_v, filt_b, value], axis=0)
        packed = shifted(packed, distance, segments)
        arrived_u = packed[:rank]
        arrived_v = packed[rank : 2 * rank]
        arrived_b = packed[2 * rank : 2 * rank + seq_total]
        arrived_value = packed[2 * rank + seq_total :]
        new_value = filter_apply(arrived_value, power, filt_u, filt_v, filt_b)
        value = jnp.where((segment >= distance) & (segment < 2 * distance), new_value, value)
        new_u = jnp.concatenate(
            [transposed(arrived_u, power) + product(transposed(arrived_u, filt_v), filt_u), filt_u], axis=0
        )
        new_v = jnp.concatenate([arrived_v, product(filt_v, power)], axis=0)
        filt_b = filter_apply(arrived_b, power, filt_u, filt_v, filt_b)
        filt_u, filt_v, filt_b = lax.optimization_barrier((new_u, new_v, filt_b))

        stored.append((smooth_u, smooth_v))
        packed = first_smoother if level == 0 else jnp.concatenate([smooth_u, smooth_v], axis=0)
        packed = shifted(packed, -distance, segments)
        arrived_u = packed[:rank]
        arrived_v = packed[rank:]
        new_u = jnp.concatenate(
            [product(arrived_u, power) + product(transposed(arrived_u, smooth_v), smooth_u), smooth_u], axis=0
        )
        new_v = jnp.concatenate([arrived_v, transposed(smooth_v, power)], axis=0)
        smooth_u, smooth_v = lax.optimization_barrier((new_u, new_v))
        level += 1
    stored.append((smooth_u, smooth_v))
    power = powers[level]

    hops = (segments + chain - 1) // chain - 1
    for hop in range(1, hops + 1):
        arrived_value = shifted(value, chain, segments)
        new_value = filter_apply(arrived_value, power, filt_u, filt_v, filt_b)
        value = jnp.where((segment >= hop * chain) & (segment < (hop + 1) * chain), new_value, value)
    entry = jnp.where(segment == 0, initial_mean, shifted(value, 1, segments))

    filtered = []
    current = entry
    for j in range(span):
        current = transposed(current, transition) * scales[j][None, :] + pushes[j]
        filtered.append(current)
    filtered = jnp.stack(filtered)
    mapped = product(
        transposed(filtered.reshape(span * seq_total, state_width), transition), transition
    ).reshape(span, seq_total, state_width)
    gaps = filtered - keeps[:, None, None] * mapped * scales[:, None, :]

    offsets = jnp.zeros((seq_total, state_width), jnp.float32)
    for j in range(last, -1, -1):
        offsets = keeps[j] * product(offsets, transition) * scales[j][None, :] + gaps[j]
    for level in range(len(stored) - 1):
        distance = 2**level
        left, right = stored[level]
        arrived = shifted(offsets, -distance, segments)
        offsets = jnp.where(
            segment + distance < segments,
            smoother_apply(arrived, powers[level], left, right, offsets),
            offsets,
        )
    left, right = stored[-1]
    for hop in range(1, hops + 1):
        arrived = shifted(offsets, -chain, segments)
        new_offsets = smoother_apply(arrived, power, left, right, offsets)
        band = segments - hop * chain
        offsets = jnp.where((segment >= band - chain) & (segment < band), new_offsets, offsets)
    current = shifted(offsets, -1, segments)

    smoothed = [None] * span
    for j in range(last, -1, -1):
        current = keeps[j] * product(current, transition) * scales[j][None, :] + gaps[j]
        smoothed[j] = current
    smoothed = jnp.stack(smoothed)

    both = jnp.stack([filtered, smoothed])
    both = lax.all_to_all(both, "state", split_axis=2, concat_axis=1, tiled=True)
    return (both[0], both[1])


def solution(mesh):
    return jax.shard_map(
        per_device,
        mesh=mesh,
        in_specs=(P("state", None), P(), P(), P("tm", None), P("tm"), P("tm")),
        out_specs=(P("tm", "state", None), P("tm", "state", None)),
        check_vma=False,
    )
```

```python
import jax
import jax.numpy as jnp
from jax import lax
from jax.sharding import PartitionSpec as P

AXES = ("tm", "state")


def product(left, right):
    return jnp.dot(left, right, precision=lax.Precision.HIGHEST, preferred_element_type=jnp.float32)


def transposed(left, right):
    return lax.dot_general(
        left,
        right,
        (((1,), (1,)), ((), ())),
        precision=lax.Precision.HIGHEST,
        preferred_element_type=jnp.float32,
    )


def leading(left, right):
    return lax.dot_general(
        left,
        right,
        (((0,), (0,)), ((), ())),
        precision=lax.Precision.HIGHEST,
        preferred_element_type=jnp.float32,
    )


def paired(left, right):
    return lax.dot_general(
        left,
        right,
        (((2,), (1,)), ((0,), (0,))),
        precision=lax.Precision.HIGHEST,
        preferred_element_type=jnp.float32,
    )


def shifted(block, distance, total):
    route = [(i, i + distance) for i in range(total) if 0 <= i + distance < total]
    return lax.ppermute(block, AXES, route)


def filter_apply(rows, power, left, right, offsets):
    return transposed(rows, power) + product(transposed(rows, right), left) + offsets


def smoother_apply(rows, power, left, right, offsets):
    return product(rows, power) + product(transposed(rows, right), left) + offsets


def per_device(dynamics, pattern, initial_mean, observed, obs_index, obs_noise):
    state_width = dynamics.shape[1]
    blocks = pattern.shape[0]
    block_span = state_width // blocks
    seq_total = initial_mean.shape[0]
    members = lax.axis_size("state")
    segments = lax.axis_size("tm") * members
    member = lax.axis_index("state")
    segment = lax.axis_index(AXES)
    span = observed.shape[0] // members
    steps_total = span * segments
    last = span - 1

    present = jnp.maximum(pattern, jnp.eye(blocks, dtype=jnp.int32))
    block_mask = jnp.repeat(jnp.repeat(present, block_span, 0), block_span, 1).astype(jnp.float32)
    pieces = [dynamics]
    for step in range(1, members):
        route = [(i, (i + step) % members) for i in range(members)]
        pieces.append(lax.ppermute(dynamics, "state", route))
    order = (member - jnp.arange(members, dtype=jnp.int32)) % members
    gathered = jnp.take(jnp.stack(pieces), order, axis=0).reshape(state_width, state_width)
    transition = gathered * block_mask

    first = member * span
    obs_here = lax.dynamic_slice_in_dim(observed, first, span, 0)
    index_here = lax.dynamic_slice_in_dim(obs_index, first, span, 0)
    noise_here = lax.dynamic_slice_in_dim(obs_noise, first, span, 0)
    gains = 1.0 / (1.0 + noise_here)
    state_index = jnp.arange(state_width, dtype=jnp.int32)
    hits = (state_index[None, :] == index_here[:, None]).astype(jnp.float32)
    scales = 1.0 - gains[:, None] * hits
    global_step = segment * span + jnp.arange(span, dtype=jnp.int32)
    keeps = jnp.where(global_step == steps_total - 1, 0.0, 1.0).astype(jnp.float32)
    pushes = [(gains[j] * obs_here[j])[:, None] * hits[j][None, :] for j in range(span)]
    column = jnp.arange(span, dtype=jnp.int32)[:, None]

    chain = max(1, segments // 4)
    powers = []
    power = transition
    length = 1
    while length < span:
        power = product(power, power)
        length *= 2
    powers.append(power)
    while len(powers) < chain.bit_length():
        power = product(power, power)
        powers.append(power)

    pair = jnp.stack([transition, transition.T])
    hit_columns = hits.T
    current = jnp.stack([hit_columns, hit_columns])
    moved = [current]
    for _ in range(last):
        current = paired(pair, current)
        moved.append(current)
    filt_u = jnp.stack([-gains[j] * moved[last - j][0, :, j] for j in range(span)], axis=0)
    smooth_u = jnp.stack([-gains[j] * moved[j][1, :, j] for j in range(span)], axis=0)
    reach = paired(jnp.stack([hits, hits]), pair)
    for turn in range(last):
        later, earlier = last - 1 - turn, 1 + turn
        scaled = jnp.stack([reach[0] * scales[later][None, :], reach[1] * scales[earlier][None, :]])
        moved_rows = paired(scaled, pair)
        reach = jnp.stack(
            [
                jnp.where(column > later, moved_rows[0], reach[0]),
                jnp.where(column < earlier, moved_rows[1], reach[1]),
            ]
        )
    filt_v, smooth_v = reach[0], reach[1]
    sweep = jnp.concatenate([jnp.zeros_like(initial_mean), initial_mean], axis=0)
    for j in range(span):
        sweep = transposed(sweep, transition) * scales[j][None, :] + jnp.concatenate([pushes[j], pushes[j]], axis=0)
    filt_b, value = sweep[:seq_total], sweep[seq_total:]

    stored = []
    level = 0
    while 2**level < chain:
        distance = 2**level
        power = powers[level]
        rank = filt_u.shape[0]
        packed = jnp.concatenate([filt_u, filt_v, filt_b, value], axis=0)
        packed = shifted(packed, distance, segments)
        arrived_u = packed[:rank]
        arrived_v = packed[rank : 2 * rank]
        arrived_b = packed[2 * rank : 2 * rank + seq_total]
        arrived_value = packed[2 * rank + seq_total :]
        new_value = filter_apply(arrived_value, power, filt_u, filt_v, filt_b)
        value = jnp.where((segment >= distance) & (segment < 2 * distance), new_value, value)
        new_u = jnp.concatenate(
            [transposed(arrived_u, power) + product(transposed(arrived_u, filt_v), filt_u), filt_u], axis=0
        )
        new_v = jnp.concatenate([arrived_v, product(filt_v, power)], axis=0)
        filt_b = filter_apply(arrived_b, power, filt_u, filt_v, filt_b)
        filt_u, filt_v, filt_b = lax.optimization_barrier((new_u, new_v, filt_b))

        stored.append((smooth_u, smooth_v))
        packed = shifted(jnp.concatenate([smooth_u, smooth_v], axis=0), -distance, segments)
        arrived_u = packed[:rank]
        arrived_v = packed[rank:]
        new_u = jnp.concatenate(
            [product(arrived_u, power) + product(transposed(arrived_u, smooth_v), smooth_u), smooth_u], axis=0
        )
        new_v = jnp.concatenate([arrived_v, transposed(smooth_v, power)], axis=0)
        smooth_u, smooth_v = lax.optimization_barrier((new_u, new_v))
        level += 1
    stored.append((smooth_u, smooth_v))
    power = powers[level]

    hops = (segments + chain - 1) // chain - 1
    for hop in range(1, hops + 1):
        arrived_value = shifted(value, chain, segments)
        new_value = filter_apply(arrived_value, power, filt_u, filt_v, filt_b)
        value = jnp.where((segment >= hop * chain) & (segment < (hop + 1) * chain), new_value, value)
    entry = jnp.where(segment == 0, initial_mean, shifted(value, 1, segments))

    filtered = []
    current = entry
    for j in range(span):
        current = transposed(current, transition) * scales[j][None, :] + pushes[j]
        filtered.append(current)
    filtered = jnp.stack(filtered)
    placed_filtered = lax.all_to_all(filtered, "state", split_axis=1, concat_axis=0, tiled=True)
    mapped = product(
        transposed(filtered.reshape(span * seq_total, state_width), transition), transition
    ).reshape(span, seq_total, state_width)
    gaps = filtered - keeps[:, None, None] * mapped * scales[:, None, :]

    offsets = jnp.zeros((seq_total, state_width), jnp.float32)
    for j in range(last, -1, -1):
        offsets = keeps[j] * product(offsets, transition) * scales[j][None, :] + gaps[j]
    for level in range(len(stored) - 1):
        distance = 2**level
        left, right = stored[level]
        arrived = shifted(offsets, -distance, segments)
        offsets = jnp.where(
            segment + distance < segments,
            smoother_apply(arrived, powers[level], left, right, offsets),
            offsets,
        )
    left, right = stored[-1]
    for hop in range(1, hops + 1):
        arrived = shifted(offsets, -chain, segments)
        new_offsets = smoother_apply(arrived, power, left, right, offsets)
        band = segments - hop * chain
        offsets = jnp.where((segment >= band - chain) & (segment < band), new_offsets, offsets)
    current = shifted(offsets, -1, segments)

    smoothed = [None] * span
    for j in range(last, -1, -1):
        current = keeps[j] * product(current, transition) * scales[j][None, :] + gaps[j]
        smoothed[j] = current
    smoothed = jnp.stack(smoothed)

    smoothed = lax.all_to_all(smoothed, "state", split_axis=1, concat_axis=0, tiled=True)
    return (placed_filtered, smoothed)


def solution(mesh):
    return jax.shard_map(
        per_device,
        mesh=mesh,
        in_specs=(P("state", None), P(), P(), P("tm", None), P("tm"), P("tm")),
        out_specs=(P("tm", "state", None), P("tm", "state", None)),
        check_vma=False,
    )
```

```python
import jax
import jax.numpy as jnp
from jax import lax
from jax.sharding import PartitionSpec as P

AXES = ("tm", "state")


def product(left, right):
    return jnp.dot(left, right, precision=lax.Precision.HIGHEST, preferred_element_type=jnp.float32)


def transposed(left, right):
    return lax.dot_general(
        left,
        right,
        (((1,), (1,)), ((), ())),
        precision=lax.Precision.HIGHEST,
        preferred_element_type=jnp.float32,
    )


def leading(left, right):
    return lax.dot_general(
        left,
        right,
        (((0,), (0,)), ((), ())),
        precision=lax.Precision.HIGHEST,
        preferred_element_type=jnp.float32,
    )


def paired(left, right):
    return lax.dot_general(
        left,
        right,
        (((2,), (1,)), ((0,), (0,))),
        precision=lax.Precision.HIGHEST,
        preferred_element_type=jnp.float32,
    )


def shifted(block, distance, total):
    route = [(i, i + distance) for i in range(total) if 0 <= i + distance < total]
    return lax.ppermute(block, AXES, route)


def filter_apply(rows, power, left, right, offsets):
    return transposed(rows, power) + product(transposed(rows, right), left) + offsets


def smoother_apply(rows, power, left, right, offsets):
    return product(rows, power) + product(transposed(rows, right), left) + offsets


def per_device(dynamics, pattern, initial_mean, observed, obs_index, obs_noise):
    state_width = dynamics.shape[1]
    blocks = pattern.shape[0]
    block_span = state_width // blocks
    seq_total = initial_mean.shape[0]
    members = lax.axis_size("state")
    segments = lax.axis_size("tm") * members
    member = lax.axis_index("state")
    segment = lax.axis_index(AXES)
    span = observed.shape[0] // members
    steps_total = span * segments
    last = span - 1

    present = jnp.maximum(pattern, jnp.eye(blocks, dtype=jnp.int32))
    block_mask = jnp.repeat(jnp.repeat(present, block_span, 0), block_span, 1).astype(jnp.float32)
    pieces = [dynamics]
    for step in range(1, members):
        route = [(i, (i + step) % members) for i in range(members)]
        pieces.append(lax.ppermute(dynamics, "state", route))
    order = (member - jnp.arange(members, dtype=jnp.int32)) % members
    gathered = jnp.take(jnp.stack(pieces), order, axis=0).reshape(state_width, state_width)
    transition = gathered * block_mask

    first = member * span
    obs_here = lax.dynamic_slice_in_dim(observed, first, span, 0)
    index_here = lax.dynamic_slice_in_dim(obs_index, first, span, 0)
    noise_here = lax.dynamic_slice_in_dim(obs_noise, first, span, 0)
    gains = 1.0 / (1.0 + noise_here)
    state_index = jnp.arange(state_width, dtype=jnp.int32)
    hits = (state_index[None, :] == index_here[:, None]).astype(jnp.float32)
    scales = 1.0 - gains[:, None] * hits
    global_step = segment * span + jnp.arange(span, dtype=jnp.int32)
    keeps = jnp.where(global_step == steps_total - 1, 0.0, 1.0).astype(jnp.float32)
    pushes = [(gains[j] * obs_here[j])[:, None] * hits[j][None, :] for j in range(span)]
    column = jnp.arange(span, dtype=jnp.int32)[:, None]

    chain = max(1, segments // 2)
    powers = []
    power = transition
    length = 1
    while length < span:
        power = product(power, power)
        length *= 2
    powers.append(power)
    while len(powers) < chain.bit_length():
        power = product(power, power)
        powers.append(power)

    pair = jnp.stack([transition, transition.T])
    hit_columns = hits.T
    current = jnp.stack([hit_columns, hit_columns])
    moved = [current]
    for _ in range(last):
        current = paired(pair, current)
        moved.append(current)
    filt_u = jnp.stack([-gains[j] * moved[last - j][0, :, j] for j in range(span)], axis=0)
    smooth_u = jnp.stack([-gains[j] * moved[j][1, :, j] for j in range(span)], axis=0)
    reach = paired(jnp.stack([hits, hits]), pair)
    for turn in range(last):
        later, earlier = last - 1 - turn, 1 + turn
        scaled = jnp.stack([reach[0] * scales[later][None, :], reach[1] * scales[earlier][None, :]])
        moved_rows = paired(scaled, pair)
        reach = jnp.stack(
            [
                jnp.where(column > later, moved_rows[0], reach[0]),
                jnp.where(column < earlier, moved_rows[1], reach[1]),
            ]
        )
    filt_v, smooth_v = reach[0], reach[1]
    sweep = jnp.concatenate([jnp.zeros_like(initial_mean), initial_mean], axis=0)
    for j in range(span):
        sweep = transposed(sweep, transition) * scales[j][None, :] + jnp.concatenate([pushes[j], pushes[j]], axis=0)
    filt_b, value = sweep[:seq_total], sweep[seq_total:]

    stored = []
    level = 0
    while 2**level < chain:
        distance = 2**level
        power = powers[level]
        rank = filt_u.shape[0]
        packed = jnp.concatenate([filt_u, filt_v, filt_b, value], axis=0)
        packed = shifted(packed, distance, segments)
        arrived_u = packed[:rank]
        arrived_v = packed[rank : 2 * rank]
        arrived_b = packed[2 * rank : 2 * rank + seq_total]
        arrived_value = packed[2 * rank + seq_total :]
        new_value = filter_apply(arrived_value, power, filt_u, filt_v, filt_b)
        value = jnp.where((segment >= distance) & (segment < 2 * distance), new_value, value)
        new_u = jnp.concatenate(
            [transposed(arrived_u, power) + product(transposed(arrived_u, filt_v), filt_u), filt_u], axis=0
        )
        new_v = jnp.concatenate([arrived_v, product(filt_v, power)], axis=0)
        filt_b = filter_apply(arrived_b, power, filt_u, filt_v, filt_b)
        filt_u, filt_v, filt_b = lax.optimization_barrier((new_u, new_v, filt_b))

        stored.append((smooth_u, smooth_v))
        packed = shifted(jnp.concatenate([smooth_u, smooth_v], axis=0), -distance, segments)
        arrived_u = packed[:rank]
        arrived_v = packed[rank:]
        new_u = jnp.concatenate(
            [product(arrived_u, power) + product(transposed(arrived_u, smooth_v), smooth_u), smooth_u], axis=0
        )
        new_v = jnp.concatenate([arrived_v, transposed(smooth_v, power)], axis=0)
        smooth_u, smooth_v = lax.optimization_barrier((new_u, new_v))
        level += 1
    stored.append((smooth_u, smooth_v))
    power = powers[level]

    hops = (segments + chain - 1) // chain - 1
    for hop in range(1, hops + 1):
        arrived_value = shifted(value, chain, segments)
        new_value = filter_apply(arrived_value, power, filt_u, filt_v, filt_b)
        value = jnp.where((segment >= hop * chain) & (segment < (hop + 1) * chain), new_value, value)
    entry = jnp.where(segment == 0, initial_mean, shifted(value, 1, segments))

    filtered = []
    current = entry
    for j in range(span):
        current = transposed(current, transition) * scales[j][None, :] + pushes[j]
        filtered.append(current)
    filtered = jnp.stack(filtered)
    mapped = product(
        transposed(filtered.reshape(span * seq_total, state_width), transition), transition
    ).reshape(span, seq_total, state_width)
    gaps = filtered - keeps[:, None, None] * mapped * scales[:, None, :]

    offsets = jnp.zeros((seq_total, state_width), jnp.float32)
    for j in range(last, -1, -1):
        offsets = keeps[j] * product(offsets, transition) * scales[j][None, :] + gaps[j]
    for level in range(len(stored) - 1):
        distance = 2**level
        left, right = stored[level]
        arrived = shifted(offsets, -distance, segments)
        offsets = jnp.where(
            segment + distance < segments,
            smoother_apply(arrived, powers[level], left, right, offsets),
            offsets,
        )
    left, right = stored[-1]
    for hop in range(1, hops + 1):
        arrived = shifted(offsets, -chain, segments)
        new_offsets = smoother_apply(arrived, power, left, right, offsets)
        band = segments - hop * chain
        offsets = jnp.where((segment >= band - chain) & (segment < band), new_offsets, offsets)
    current = shifted(offsets, -1, segments)

    smoothed = [None] * span
    for j in range(last, -1, -1):
        current = keeps[j] * product(current, transition) * scales[j][None, :] + gaps[j]
        smoothed[j] = current
    smoothed = jnp.stack(smoothed)

    both = jnp.stack([filtered, smoothed])
    both = lax.all_to_all(both, "state", split_axis=2, concat_axis=1, tiled=True)
    return (both[0], both[1])


def solution(mesh):
    return jax.shard_map(
        per_device,
        mesh=mesh,
        in_specs=(P("state", None), P(), P(), P("tm", None), P("tm"), P("tm")),
        out_specs=(P("tm", "state", None), P("tm", "state", None)),
        check_vma=False,
    )
```
